256 devices in a mesh: sta: 256 (over y, z, x, core).
Axes of the slice: x: 4, y: 4, z: 8, core: 2. Of those that a mesh axis runs over, the one named last changes fastest.
Arguments:
- records: bfloat16 [20480, 2048], P('sta'), may hold values from -6 to 6
- green: bfloat16 [20480, 2048], P('sta'), may hold values from -4 to 4
- pair_mask: int32 [20480, 720], P('sta'), may hold values 0 or 1
- tile_lists: int32 [20480, 16], P('sta'), may hold values from 0 to 1023
- tile_weights: float32 [20480, 16], P('sta'), may hold values from -0.3125 to 0.3125
- tile_green: bfloat16 [524288, 1024], P('sta'), may hold values from -0.125 to 0.125
Outputs:
- adjoint: bfloat16 [20480, 2048], P('sta')
- kernel: float32 [1024, 1024], P('sta')
The draws below stay inside these ranges and needn't reach their ends.
All inputs are finite; a program needn't handle non-finite values. No bound on the sum of `pair_mask` on one device may be relied on, other than what follows from the above.
Results may differ from the reference program's by a relative error of at most 0.0034.
Values may be sent and summed in bfloat16 or wider, within the bound.
No kernel may reach another device: no remote copies, remote signals or barrier semaphores. Data moves between devices by JAX's collectives and lax.ppermute only.
A program may use at most 64 MiB of HBM per device.

```python
import jax
import jax.numpy as jnp
from jax import lax

C = 80
F = 1024
CT = 1024
TT = 4
L = 16
HALF = 4
WIN = 9
CHANNELS = 20480
TILES = 1024
N_STA = 256


def place_ends(values, stream_key, smallest, top_value):
    extent = values.shape
    spot = [jax.random.randint(jax.random.fold_in(stream_key, axis), (), 0, extent[axis]) for axis in range(len(extent))]
    values = values.at[tuple(spot)].set(smallest)
    longest = extent.index(max(extent))
    spot[longest] = (spot[longest] + 1) % extent[longest]
    return values.at[tuple(spot)].set(top_value)


def block_scale(own_key, extent, shards, least, high):
    def one(position, blocks):
        steps = jax.random.uniform(jax.random.fold_in(jax.random.fold_in(own_key, 6), position), (blocks,), jnp.float32, least / len(shards), high / len(shards))
        return jnp.repeat(jnp.exp(steps), extent[position] // blocks).reshape((-1,) + (1,) * (len(extent) - position - 1))

    gain = one(*shards[0])
    for cut in shards[1:]:
        gain = gain * one(*cut)
    return gain


def bell_draw(key, extent, width, limit, shards=(), kind=jnp.bfloat16):
    result = jax.random.normal(key, extent, jnp.float32) * width
    if len(shards) > 0:
        result = block_scale(key, extent, shards, -0.22, 0.18) * result
    return jnp.clip(result, min=-limit, max=limit).astype(kind)


def setup_inputs(seed: int = 0) -> dict:
    key_list = jax.random.split(jax.random.key(seed), 7)
    records = bell_draw(key_list[0], (CHANNELS, 2 * F), 1.0, 6.0, ((0, 256),))
    green = bell_draw(key_list[1], (CHANNELS, 2 * F), 0.6, 4.0, ((0, 256),))
    pair_mask = place_ends((jax.random.randint(key_list[2], (CHANNELS, WIN * C), 0, 2) < 1).astype(jnp.int32), jax.random.fold_in(key_list[2], 1), 0, 1)
    tile_lists = place_ends(jax.random.randint(key_list[3], (CHANNELS, L), 0, TILES), jax.random.fold_in(key_list[3], 1), 0, TILES - 1).astype(jnp.int32)
    tile_weights = bell_draw(key_list[4], (CHANNELS, L), (C * L // TT) ** -0.5, 0.3125, ((0, 256),), jnp.float32)
    tile_green = bell_draw(key_list[5], (2 * F * N_STA, CT), (2 * F) ** -0.5, 0.125, ((0, 256),))
    return {"records": records, "green": green, "pair_mask": pair_mask, "tile_lists": tile_lists, "tile_weights": tile_weights, "tile_green": tile_green}


def reference(records, green, pair_mask, tile_lists, tile_weights, tile_green):
    blocks = N_STA
    rec = records.astype(jnp.float32)
    grn = green.astype(jnp.float32)
    rec_real, rec_imag = (rec[:, :F], rec[:, F:])
    green_real, green_imag = (grn[:, :F], grn[:, F:])
    cross = jnp.concatenate([rec_real * green_real + rec_imag * green_imag, rec_real * green_imag - rec_imag * green_real], axis=1).astype(jnp.bfloat16)
    power = (green_real * green_real + green_imag * green_imag).astype(jnp.bfloat16)
    cross_blocks = cross.astype(jnp.float32).reshape(blocks, C, 2 * F)
    power_blocks = power.astype(jnp.float32).reshape(blocks, C, F)
    mask_blocks = pair_mask.astype(jnp.float32).reshape(blocks, C, WIN, C)
    qsum = jnp.zeros((blocks, C, 2 * F), jnp.float32)
    psum = jnp.zeros((blocks, C, F), jnp.float32)
    for offset in range(WIN):
        rolled_cross = jnp.roll(cross_blocks, HALF - offset, axis=0)
        rolled_power = jnp.roll(power_blocks, HALF - offset, axis=0)
        qsum = qsum + jnp.einsum('bic,bcf->bif', mask_blocks[:, :, offset, :], rolled_cross, precision=lax.Precision.HIGHEST)
        psum = psum + jnp.einsum('bic,bcf->bif', mask_blocks[:, :, offset, :], rolled_power, precision=lax.Precision.HIGHEST)
    factor = 1.0 / jnp.sqrt(jnp.float32(WIN * C))
    qsum = (qsum * factor).reshape(blocks * C, 2 * F)
    psum = (psum * factor).reshape(blocks * C, F)
    q_real, q_imag = (qsum[:, :F], qsum[:, F:])
    adj_real = rec_real * q_real - rec_imag * q_imag - green_real * psum
    adj_imag = rec_real * q_imag + rec_imag * q_real - green_imag * psum
    adjoint = jnp.concatenate([adj_real, adj_imag], axis=1).astype(jnp.bfloat16)
    tiles_total = TT * blocks
    tile_ids = jnp.arange(tiles_total, dtype=jnp.int32)

    def one_block(total, inputs):
        adj_rows, lists_rows, weight_rows, green_rows = inputs
        onehot = (lists_rows[None, :, :] == tile_ids[:, None, None]).astype(jnp.float32)
        tile_map = lax.optimization_barrier(jnp.sum(onehot * weight_rows[None, :, :], axis=2))
        spread = jnp.dot(tile_map, adj_rows.astype(jnp.float32), precision=lax.Precision.HIGHEST)
        return (total + jnp.dot(spread, green_rows.astype(jnp.float32), precision=lax.Precision.HIGHEST), None)
    inputs = (adjoint.reshape(blocks, C, 2 * F), tile_lists.reshape(blocks, C, L), tile_weights.reshape(blocks, C, L), tile_green.reshape(blocks, 2 * F, CT))
    kernel, unused = lax.scan(one_block, jnp.zeros((tiles_total, CT), jnp.float32), inputs)
    return (adjoint, kernel)
```

```python
import numpy as np
import jax
import jax.numpy as jnp
from jax import lax
from jax.sharding import Mesh
from jax.sharding import PartitionSpec as P

C = 80
F = 1024
TT = 4
HALF = 4
WIN = 9

SUB = ("y", "z", "x", "c")
SIZES = (4, 4, 8, 2)
RS_ORDER = ("c", "x", "z", "y")


def shifted(value, steps, count):
    pairs = [(source, (source + steps) % count) for source in range(count)]
    return lax.ppermute(value, SUB, pairs)


def tile_order():
    y, z, x, c, i = np.meshgrid(
        *[np.arange(n) for n in SIZES], np.arange(TT), indexing="ij"
    )
    flat = (((y * SIZES[1] + z) * SIZES[2] + x) * SIZES[3] + c) * TT + i
    perm = [SUB.index(a) for a in RS_ORDER] + [4]
    return flat.transpose(perm).reshape(-1).astype(np.int32)


def local(records, green, pair_mask, tile_lists, tile_weights, tile_green):
    count = int(np.prod(SIZES))
    rec = records.astype(jnp.float32)
    grn = green.astype(jnp.float32)
    rec_real, rec_imag = (rec[:, :F], rec[:, F:])
    green_real, green_imag = (grn[:, :F], grn[:, F:])
    both = jnp.concatenate(
        [
            rec_real * green_real + rec_imag * green_imag,
            rec_real * green_imag - rec_imag * green_real,
            green_real * green_real + green_imag * green_imag,
        ],
        axis=1,
    ).astype(jnp.bfloat16)
    mask_bf = pair_mask.astype(jnp.bfloat16)
    total = jnp.dot(
        mask_bf[:, HALF * C : (HALF + 1) * C], both, preferred_element_type=jnp.float32
    )
    for offset in range(WIN):
        if offset == HALF:
            continue
        moving = shifted(both, HALF - offset, count)
        columns = mask_bf[:, offset * C : (offset + 1) * C]
        total = total + jnp.dot(columns, moving, preferred_element_type=jnp.float32)
    factor = 1.0 / jnp.sqrt(jnp.float32(WIN * C))
    total = total * factor
    q_real, q_imag, psum = (total[:, :F], total[:, F : 2 * F], total[:, 2 * F :])
    adj_real = rec_real * q_real - rec_imag * q_imag - green_real * psum
    adj_imag = rec_real * q_imag + rec_imag * q_real - green_imag * psum
    adjoint = jnp.concatenate([adj_real, adj_imag], axis=1).astype(jnp.bfloat16)
    response = jnp.dot(adjoint, tile_green, preferred_element_type=jnp.float32)
    tile_ids = jnp.asarray(tile_order())
    onehot = (tile_lists[None, :, :] == tile_ids[:, None, None]).astype(jnp.float32)
    tile_map = jnp.sum(onehot * tile_weights[None, :, :], axis=2)
    part = jnp.dot(tile_map, response, precision=lax.Precision.HIGHEST)
    for axis in RS_ORDER:
        part = lax.psum_scatter(part, axis, scatter_dimension=0, tiled=True)
    return (adjoint, part)


def solution(mesh):
    devices = np.asarray(mesh.devices).reshape(SIZES)
    grid = Mesh(devices, SUB)
    rows = P(SUB, None)
    return jax.shard_map(
        local,
        mesh=grid,
        in_specs=(rows,) * 6,
        out_specs=(rows, rows),
        check_vma=False,
    )
```

```python
import numpy as np
import jax
import jax.numpy as jnp
from jax import lax
from jax.sharding import Mesh
from jax.sharding import PartitionSpec as P

C = 80
F = 1024
TT = 4
HALF = 4
WIN = 9

SUB = ("y", "z", "x", "c")
SIZES = (4, 4, 8, 2)
RS_ORDER = ("c", "x", "z", "y")


def shifted(value, steps, count):
    pairs = [(source, (source + steps) % count) for source in range(count)]
    return lax.ppermute(value, SUB, pairs)


def swap(value, count):
    pairs = [(source, source ^ 1) for source in range(count)]
    return lax.ppermute(value, SUB, pairs)


def tile_order():
    y, z, x, c, i = np.meshgrid(
        *[np.arange(n) for n in SIZES], np.arange(TT), indexing="ij"
    )
    flat = (((y * SIZES[1] + z) * SIZES[2] + x) * SIZES[3] + c) * TT + i
    perm = [SUB.index(a) for a in RS_ORDER] + [4]
    return flat.transpose(perm).reshape(-1).astype(np.int32)


def local(records, green, pair_mask, tile_lists, tile_weights, tile_green):
    count = int(np.prod(SIZES))
    rec = records.astype(jnp.float32)
    grn = green.astype(jnp.float32)
    rec_real, rec_imag = (rec[:, :F], rec[:, F:])
    green_real, green_imag = (grn[:, :F], grn[:, F:])
    both = jnp.concatenate(
        [
            rec_real * green_real + rec_imag * green_imag,
            rec_real * green_imag - rec_imag * green_real,
            green_real * green_real + green_imag * green_imag,
        ],
        axis=1,
    ).astype(jnp.bfloat16)
    mask_bf = pair_mask.astype(jnp.bfloat16)
    first = lax.axis_index(SUB) % 2 == 0

    def cols(offset):
        return mask_bf[:, offset * C : (offset + 1) * C]

    def picked(on_first, on_second):
        return jnp.where(first, cols(on_first), cols(on_second))

    def add(total, columns, moving):
        return total + jnp.dot(columns, moving, preferred_element_type=jnp.float32)

    ahead = shifted(both, -2, count)
    behind = shifted(both, 2, count)
    total = jnp.dot(cols(HALF), both, preferred_element_type=jnp.float32)
    total = add(total, cols(HALF + 2), ahead)
    total = add(total, cols(HALF - 2), behind)
    ahead2 = shifted(ahead, -2, count)
    behind2 = shifted(behind, 2, count)
    width = both.shape[1]
    swapped = swap(jnp.concatenate([both, ahead, behind], axis=1), count)
    total = add(total, picked(HALF + 1, HALF - 1), swapped[:, :width])
    total = add(total, picked(HALF + 3, HALF + 1), swapped[:, width : 2 * width])
    total = add(total, picked(HALF - 1, HALF - 3), swapped[:, 2 * width :])
    total = add(total, cols(HALF + 4), ahead2)
    total = add(total, cols(HALF - 4), behind2)
    last = swap(jnp.where(first, ahead2, behind2), count)
    total = add(total, picked(HALF - 3, HALF + 3), last)
    factor = 1.0 / jnp.sqrt(jnp.float32(WIN * C))
    total = total * factor
    q_real, q_imag, psum = (total[:, :F], total[:, F : 2 * F], total[:, 2 * F :])
    adj_real = rec_real * q_real - rec_imag * q_imag - green_real * psum
    adj_imag = rec_real * q_imag + rec_imag * q_real - green_imag * psum
    adjoint = jnp.concatenate([adj_real, adj_imag], axis=1).astype(jnp.bfloat16)
    response = jnp.dot(adjoint, tile_green, preferred_element_type=jnp.float32)
    tile_ids = jnp.asarray(tile_order())
    onehot = (tile_lists[None, :, :] == tile_ids[:, None, None]).astype(jnp.float32)
    tile_map = jnp.sum(onehot * tile_weights[None, :, :], axis=2)
    part = jnp.dot(tile_map, response, precision=lax.Precision.HIGHEST)
    part = part.reshape(SIZES[SUB.index(RS_ORDER[0])], -1, part.shape[1])
    part = jnp.sum(lax.all_to_all(part, RS_ORDER[0], 0, 0, tiled=False), axis=0)
    part = part.reshape(-1, TT, part.shape[1])
    part = lax.all_to_all(part, RS_ORDER[1:], 0, 0, tiled=False)
    return (adjoint, jnp.sum(part, axis=0))


def solution(mesh):
    devices = np.asarray(mesh.devices).reshape(SIZES)
    grid = Mesh(devices, SUB)
    rows = P(SUB, None)
    return jax.shard_map(
        local,
        mesh=grid,
        in_specs=(rows,) * 6,
        out_specs=(rows, rows),
        check_vma=False,
    )
```

```python
import numpy as np
import jax
import jax.numpy as jnp
from jax import lax
from jax.sharding import Mesh
from jax.sharding import PartitionSpec as P

C = 80
F = 1024
TT = 4
HALF = 4
WIN = 9

SUB = ("y", "z", "x", "c")
SIZES = (4, 4, 8, 2)
RS_ORDER = ("c", "x", "z", "y")
STAGES = (("x",), ("z", "y"))


def shifted(value, steps, count):
    pairs = [(source, (source + steps) % count) for source in range(count)]
    return lax.ppermute(value, SUB, pairs)


def swap(value, count):
    pairs = [(source, source ^ 1) for source in range(count)]
    return lax.ppermute(value, SUB, pairs)


def tile_order():
    y, z, x, c, i = np.meshgrid(
        *[np.arange(n) for n in SIZES], np.arange(TT), indexing="ij"
    )
    flat = (((y * SIZES[1] + z) * SIZES[2] + x) * SIZES[3] + c) * TT + i
    perm = [SUB.index(a) for a in RS_ORDER] + [4]
    return flat.transpose(perm).reshape(-1).astype(np.int32)


def local(records, green, pair_mask, tile_lists, tile_weights, tile_green):
    count = int(np.prod(SIZES))
    rec = records.astype(jnp.float32)
    grn = green.astype(jnp.float32)
    rec_real, rec_imag = (rec[:, :F], rec[:, F:])
    green_real, green_imag = (grn[:, :F], grn[:, F:])
    both = jnp.concatenate(
        [
            rec_real * green_real + rec_imag * green_imag,
            rec_real * green_imag - rec_imag * green_real,
            green_real * green_real + green_imag * green_imag,
        ],
        axis=1,
    ).astype(jnp.bfloat16)
    mask_bf = pair_mask.astype(jnp.bfloat16)
    first = lax.axis_index(SUB) % 2 == 0

    def cols(offset):
        return mask_bf[:, offset * C : (offset + 1) * C]

    def picked(on_first, on_second):
        return jnp.where(first, cols(on_first), cols(on_second))

    def add(total, columns, moving):
        return total + jnp.dot(columns, moving, preferred_element_type=jnp.float32)

    ahead = shifted(both, -2, count)
    behind = shifted(both, 2, count)
    total = jnp.dot(cols(HALF), both, preferred_element_type=jnp.float32)
    total = add(total, cols(HALF + 2), ahead)
    total = add(total, cols(HALF - 2), behind)
    ahead2 = shifted(ahead, -2, count)
    behind2 = shifted(behind, 2, count)
    width = both.shape[1]
    swapped = swap(jnp.concatenate([both, ahead, behind], axis=1), count)
    total = add(total, picked(HALF + 1, HALF - 1), swapped[:, :width])
    total = add(total, picked(HALF + 3, HALF + 1), swapped[:, width : 2 * width])
    total = add(total, picked(HALF - 1, HALF - 3), swapped[:, 2 * width :])
    total = add(total, cols(HALF + 4), ahead2)
    total = add(total, cols(HALF - 4), behind2)
    last = swap(jnp.where(first, ahead2, behind2), count)
    total = add(total, picked(HALF - 3, HALF + 3), last)
    factor = 1.0 / jnp.sqrt(jnp.float32(WIN * C))
    total = total * factor
    q_real, q_imag, psum = (total[:, :F], total[:, F : 2 * F], total[:, 2 * F :])
    adj_real = rec_real * q_real - rec_imag * q_imag - green_real * psum
    adj_imag = rec_real * q_imag + rec_imag * q_real - green_imag * psum
    adjoint = jnp.concatenate([adj_real, adj_imag], axis=1).astype(jnp.bfloat16)
    response = jnp.dot(adjoint, tile_green, preferred_element_type=jnp.float32)
    responses = jnp.concatenate([response, swap(response, count)], axis=0)
    lists = jnp.concatenate([tile_lists, swap(tile_lists, count)], axis=0)
    weights = jnp.concatenate([tile_weights, swap(tile_weights, count)], axis=0)
    tile_ids = jnp.asarray(tile_order()[: TT * count // SIZES[-1]]) + TT * (lax.axis_index(SUB) % 2)
    onehot = (lists[None, :, :] == tile_ids[:, None, None]).astype(jnp.float32)
    tile_map = jnp.sum(onehot * weights[None, :, :], axis=2)
    part = jnp.dot(tile_map, responses, precision=lax.Precision.HIGHEST)
    for group in STAGES:
        ways = int(np.prod([SIZES[SUB.index(a)] for a in group]))
        part = part.reshape(ways, -1, part.shape[1])
        part = jnp.sum(lax.all_to_all(part, group, 0, 0, tiled=False), axis=0)
    return (adjoint, part)


def solution(mesh):
    devices = np.asarray(mesh.devices).reshape(SIZES)
    grid = Mesh(devices, SUB)
    rows = P(SUB, None)
    return jax.shard_map(
        local,
        mesh=grid,
        in_specs=(rows,) * 6,
        out_specs=(rows, rows),
        check_vma=False,
    )
```

```python
import numpy as np
import jax
import jax.numpy as jnp
from jax import lax
from jax.sharding import Mesh
from jax.sharding import PartitionSpec as P

C = 80
F = 1024
TT = 4
HALF = 4
WIN = 9

SUB = ("y", "z", "x", "c")
SIZES = (4, 4, 8, 2)
RS_ORDER = ("c", "x", "z", "y")
STAGES = (("x",), ("z", "y"))


def shifted(value, steps, count):
    pairs = [(source, (source + steps) % count) for source in range(count)]
    return lax.ppermute(value, SUB, pairs)


def swap(value, count):
    pairs = [(source, source ^ 1) for source in range(count)]
    return lax.ppermute(value, SUB, pairs)


def tile_order():
    y, z, x, c, i = np.meshgrid(
        *[np.arange(n) for n in SIZES], np.arange(TT), indexing="ij"
    )
    flat = (((y * SIZES[1] + z) * SIZES[2] + x) * SIZES[3] + c) * TT + i
    perm = [SUB.index(a) for a in RS_ORDER] + [4]
    return flat.transpose(perm).reshape(-1).astype(np.int32)


def body(records, green, pair_mask, tile_lists, tile_weights, tile_green):
    count = int(np.prod(SIZES))
    rec = records.astype(jnp.float32)
    grn = green.astype(jnp.float32)
    rec_real, rec_imag = (rec[:, :F], rec[:, F:])
    green_real, green_imag = (grn[:, :F], grn[:, F:])
    both = jnp.concatenate(
        [
            rec_real * green_real + rec_imag * green_imag,
            rec_real * green_imag - rec_imag * green_real,
            green_real * green_real + green_imag * green_imag,
        ],
        axis=1,
    ).astype(jnp.bfloat16)
    mask_bf = pair_mask.astype(jnp.bfloat16)
    first = lax.axis_index(SUB) % 2 == 0

    def cols(offset):
        return mask_bf[:, offset * C : (offset + 1) * C]

    def picked(on_first, on_second):
        return jnp.where(first, cols(on_first), cols(on_second))

    def add(total, columns, moving):
        return total + jnp.dot(columns, moving, preferred_element_type=jnp.float32)

    lists = jnp.concatenate([tile_lists, swap(tile_lists, count)], axis=0)
    weights = jnp.concatenate([tile_weights, swap(tile_weights, count)], axis=0)
    ahead = shifted(both, -2, count)
    behind = shifted(both, 2, count)
    ahead2 = shifted(ahead, -2, count)
    behind2 = shifted(behind, 2, count)
    total = jnp.dot(cols(HALF), both, preferred_element_type=jnp.float32)
    total = add(total, cols(HALF + 2), ahead)
    total = add(total, cols(HALF - 2), behind)
    tile_ids = jnp.asarray(tile_order()[: TT * count // SIZES[-1]]) + TT * (
        lax.axis_index(SUB) % 2
    )
    onehot = (lists[None, :, :] == tile_ids[:, None, None]).astype(jnp.float32)
    tile_map = jnp.sum(onehot * weights[None, :, :], axis=2)
    total, tile_map = lax.optimization_barrier((total, tile_map))
    width = both.shape[1]
    swapped = swap(jnp.concatenate([both, ahead, behind], axis=1), count)
    total = add(total, picked(HALF + 1, HALF - 1), swapped[:, :width])
    total = add(total, picked(HALF + 3, HALF + 1), swapped[:, width : 2 * width])
    total = add(total, picked(HALF - 1, HALF - 3), swapped[:, 2 * width :])
    total = add(total, cols(HALF + 4), ahead2)
    total = add(total, cols(HALF - 4), behind2)
    last = swap(jnp.where(first, ahead2, behind2), count)
    total = add(total, picked(HALF - 3, HALF + 3), last)
    factor = 1.0 / jnp.sqrt(jnp.float32(WIN * C))
    total = total * factor
    q_real, q_imag, psum = (total[:, :F], total[:, F : 2 * F], total[:, 2 * F :])
    adj_real = rec_real * q_real - rec_imag * q_imag - green_real * psum
    adj_imag = rec_real * q_imag + rec_imag * q_real - green_imag * psum
    adjoint = jnp.concatenate([adj_real, adj_imag], axis=1).astype(jnp.bfloat16)
    response = jnp.dot(adjoint, tile_green, preferred_element_type=jnp.float32)
    responses = jnp.concatenate([response, swap(response, count)], axis=0)
    part = jnp.dot(tile_map, responses, precision=lax.Precision.HIGHEST)
    for group in STAGES:
        ways = int(np.prod([SIZES[SUB.index(a)] for a in group]))
        part = part.reshape(ways, -1, part.shape[1])
        part = jnp.sum(lax.all_to_all(part, group, 0, 0, tiled=False), axis=0)
    return (adjoint, part)


def solution(mesh):
    devices = np.asarray(mesh.devices).reshape(SIZES)
    grid = Mesh(devices, SUB)
    rows = P(SUB, None)
    return jax.shard_map(
        body,
        mesh=grid,
        in_specs=(rows,) * 6,
        out_specs=(rows, rows),
        check_vma=False,
    )
```

```python
import numpy as np
import jax
import jax.numpy as jnp
from jax import lax
from jax.sharding import Mesh
from jax.sharding import PartitionSpec as P

C = 80
F = 1024
TT = 4
HALF = 4
WIN = 9

SUB = ("y", "z", "x", "c")
SIZES = (4, 4, 8, 2)
RS_ORDER = ("c", "x", "z", "y")
STAGES = (("x",), ("z", "y"))
PIECES = 2


def shifted(value, steps, count):
    pairs = [(source, (source + steps) % count) for source in range(count)]
    return lax.ppermute(value, SUB, pairs)


def swap(value, count):
    pairs = [(source, source ^ 1) for source in range(count)]
    return lax.ppermute(value, SUB, pairs)


def tile_order():
    y, z, x, c, i = np.meshgrid(
        *[np.arange(n) for n in SIZES], np.arange(TT), indexing="ij"
    )
    flat = (((y * SIZES[1] + z) * SIZES[2] + x) * SIZES[3] + c) * TT + i
    perm = [SUB.index(a) for a in RS_ORDER] + [4]
    return flat.transpose(perm).reshape(-1).astype(np.int32)


def body(records, green, pair_mask, tile_lists, tile_weights, tile_green):
    count = int(np.prod(SIZES))
    rec = records.astype(jnp.float32)
    grn = green.astype(jnp.float32)
    rec_real, rec_imag = (rec[:, :F], rec[:, F:])
    green_real, green_imag = (grn[:, :F], grn[:, F:])
    both = jnp.concatenate(
        [
            rec_real * green_real + rec_imag * green_imag,
            rec_real * green_imag - rec_imag * green_real,
            green_real * green_real + green_imag * green_imag,
        ],
        axis=1,
    ).astype(jnp.bfloat16)
    mask_bf = pair_mask.astype(jnp.bfloat16)
    first = lax.axis_index(SUB) % 2 == 0

    def cols(offset):
        return mask_bf[:, offset * C : (offset + 1) * C]

    def picked(on_first, on_second):
        return jnp.where(first, cols(on_first), cols(on_second))

    def add(total, columns, moving):
        return total + jnp.dot(columns, moving, preferred_element_type=jnp.float32)

    def add_pieces(total, columns, pieces):
        start = 0
        for piece in pieces:
            rows = piece.shape[0]
            total = add(total, columns[:, start : start + rows], piece)
            start += rows
        return total

    def split(value):
        step = -(-value.shape[0] // (PIECES * 16)) * 16
        return [value[i : i + step] for i in range(0, value.shape[0], step)]

    lists = jnp.concatenate([tile_lists, swap(tile_lists, count)], axis=0)
    weights = jnp.concatenate([tile_weights, swap(tile_weights, count)], axis=0)
    ahead = [shifted(piece, -2, count) for piece in split(both)]
    behind = [shifted(piece, 2, count) for piece in split(both)]
    ahead2 = [shifted(piece, -2, count) for piece in ahead]
    behind2 = [shifted(piece, 2, count) for piece in behind]
    total = jnp.dot(cols(HALF), both, preferred_element_type=jnp.float32)
    total = add_pieces(total, cols(HALF + 2), ahead)
    total = add_pieces(total, cols(HALF - 2), behind)
    tile_ids = jnp.asarray(tile_order()[: TT * count // SIZES[-1]]) + TT * (
        lax.axis_index(SUB) % 2
    )
    onehot = (lists[None, :, :] == tile_ids[:, None, None]).astype(jnp.float32)
    tile_map = jnp.sum(onehot * weights[None, :, :], axis=2)
    total, tile_map = lax.optimization_barrier((total, tile_map))
    width = both.shape[1]
    payload = [both, jnp.concatenate(ahead, axis=0), jnp.concatenate(behind, axis=0)]
    swapped = swap(jnp.concatenate(payload, axis=1), count)
    total = add(total, picked(HALF + 1, HALF - 1), swapped[:, :width])
    total = add(total, picked(HALF + 3, HALF + 1), swapped[:, width : 2 * width])
    total = add(total, picked(HALF - 1, HALF - 3), swapped[:, 2 * width :])
    total = add_pieces(total, cols(HALF + 4), ahead2)
    total = add_pieces(total, cols(HALF - 4), behind2)
    farthest = [jnp.where(first, a, b) for a, b in zip(ahead2, behind2)]
    last = swap(jnp.concatenate(farthest, axis=0), count)
    total = add(total, picked(HALF - 3, HALF + 3), last)
    factor = 1.0 / jnp.sqrt(jnp.float32(WIN * C))
    total = total * factor
    q_real, q_imag, psum = (total[:, :F], total[:, F : 2 * F], total[:, 2 * F :])
    adj_real = rec_real * q_real - rec_imag * q_imag - green_real * psum
    adj_imag = rec_real * q_imag + rec_imag * q_real - green_imag * psum
    adjoint = jnp.concatenate([adj_real, adj_imag], axis=1).astype(jnp.bfloat16)
    response = jnp.dot(adjoint, tile_green, preferred_element_type=jnp.float32)
    responses = jnp.concatenate([response, swap(response, count)], axis=0)
    part = jnp.dot(tile_map, responses, precision=lax.Precision.HIGHEST)
    for group in STAGES:
        ways = int(np.prod([SIZES[SUB.index(a)] for a in group]))
        part = part.reshape(ways, -1, part.shape[1])
        part = jnp.sum(lax.all_to_all(part, group, 0, 0, tiled=False), axis=0)
    return (adjoint, part)


def solution(mesh):
    devices = np.asarray(mesh.devices).reshape(SIZES)
    grid = Mesh(devices, SUB)
    rows = P(SUB, None)
    return jax.shard_map(
        body,
        mesh=grid,
        in_specs=(rows,) * 6,
        out_specs=(rows, rows),
        check_vma=False,
    )
```

```python
import numpy as np
import jax
import jax.numpy as jnp
from jax import lax
from jax.sharding import Mesh
from jax.sharding import PartitionSpec as P

C = 80
F = 1024
TT = 4
HALF = 4
WIN = 9

SUB = ("y", "z", "x", "c")
SIZES = (4, 4, 8, 2)
RS_ORDER = ("c", "x", "z", "y")
STAGES = (("x",), ("z", "y"))


def shifted(value, steps, count):
    pairs = [(source, (source + steps) % count) for source in range(count)]
    return lax.ppermute(value, SUB, pairs)


def swap(value, count):
    pairs = [(source, source ^ 1) for source in range(count)]
    return lax.ppermute(value, SUB, pairs)


def tile_order():
    y, z, x, c, i = np.meshgrid(
        *[np.arange(n) for n in SIZES], np.arange(TT), indexing="ij"
    )
    flat = (((y * SIZES[1] + z) * SIZES[2] + x) * SIZES[3] + c) * TT + i
    perm = [SUB.index(a) for a in RS_ORDER] + [4]
    return flat.transpose(perm).reshape(-1).astype(np.int32)


def body(records, green, pair_mask, tile_lists, tile_weights, tile_green):
    count = int(np.prod(SIZES))
    rec = records.astype(jnp.float32)
    grn = green.astype(jnp.float32)
    rec_real, rec_imag = (rec[:, :F], rec[:, F:])
    green_real, green_imag = (grn[:, :F], grn[:, F:])
    both = jnp.concatenate(
        [
            rec_real * green_real + rec_imag * green_imag,
            rec_real * green_imag - rec_imag * green_real,
            green_real * green_real + green_imag * green_imag,
        ],
        axis=1,
    ).astype(jnp.bfloat16)
    mask_bf = pair_mask.astype(jnp.bfloat16)
    first = lax.axis_index(SUB) % 2 == 0

    def cols(offset):
        return mask_bf[:, offset * C : (offset + 1) * C]

    def picked(on_first, on_second):
        return jnp.where(first, cols(on_first), cols(on_second))

    def add(total, columns, moving):
        return total + jnp.dot(columns, moving, preferred_element_type=jnp.float32)

    lists = jnp.concatenate([tile_lists, swap(tile_lists, count)], axis=0)
    weights = jnp.concatenate([tile_weights, swap(tile_weights, count)], axis=0)
    ahead = shifted(both, -2, count)
    behind = shifted(both, 2, count)
    neighbour = swap(both, count)
    ahead2 = shifted(ahead, -2, count)
    behind2 = shifted(behind, 2, count)
    total = jnp.dot(cols(HALF), both, preferred_element_type=jnp.float32)
    total = add(total, cols(HALF + 2), ahead)
    total = add(total, cols(HALF - 2), behind)
    total = add(total, picked(HALF + 1, HALF - 1), neighbour)
    tile_ids = jnp.asarray(tile_order()[: TT * count // SIZES[-1]]) + TT * (
        lax.axis_index(SUB) % 2
    )
    onehot = (lists[None, :, :] == tile_ids[:, None, None]).astype(jnp.float32)
    tile_map = jnp.sum(onehot * weights[None, :, :], axis=2)
    total, tile_map = lax.optimization_barrier((total, tile_map))
    swapped = swap(jnp.concatenate([ahead, behind], axis=0), count)
    columns = [picked(HALF + 3, HALF + 1), picked(HALF - 1, HALF - 3)]
    total = add(total, jnp.concatenate(columns, axis=1), swapped)
    last = swap(jnp.where(first, ahead2, behind2), count)
    columns = [cols(HALF + 4), cols(HALF - 4), picked(HALF - 3, HALF + 3)]
    stacked = jnp.concatenate([ahead2, behind2, last], axis=0)
    total = add(total, jnp.concatenate(columns, axis=1), stacked)
    factor = 1.0 / jnp.sqrt(jnp.float32(WIN * C))
    total = total * factor
    q_real, q_imag, psum = (total[:, :F], total[:, F : 2 * F], total[:, 2 * F :])
    adj_real = rec_real * q_real - rec_imag * q_imag - green_real * psum
    adj_imag = rec_real * q_imag + rec_imag * q_real - green_imag * psum
    adjoint = jnp.concatenate([adj_real, adj_imag], axis=1).astype(jnp.bfloat16)
    response = jnp.dot(adjoint, tile_green, preferred_element_type=jnp.float32)
    responses = jnp.concatenate([response, swap(response, count)], axis=0)
    part = jnp.dot(tile_map, responses, precision=lax.Precision.HIGHEST)
    for group in STAGES:
        ways = int(np.prod([SIZES[SUB.index(a)] for a in group]))
        part = part.reshape(ways, -1, part.shape[1])
        part = jnp.sum(lax.all_to_all(part, group, 0, 0, tiled=False), axis=0)
    return (adjoint, part)


def solution(mesh):
    devices = np.asarray(mesh.devices).reshape(SIZES)
    grid = Mesh(devices, SUB)
    rows = P(SUB, None)
    return jax.shard_map(
        body,
        mesh=grid,
        in_specs=(rows,) * 6,
        out_specs=(rows, rows),
        check_vma=False,
    )
```

```python
import numpy as np
import jax
import jax.numpy as jnp
from jax import lax
from jax.sharding import Mesh
from jax.sharding import PartitionSpec as P

C = 80
F = 1024
TT = 4
HALF = 4
WIN = 9

SUB = ("y", "z", "x", "c")
SIZES = (4, 4, 8, 2)
RS_ORDER = ("c", "x", "z", "y")
STAGES = (("x",), ("z", "y"))


def shifted(value, steps, count):
    pairs = [(source, (source + steps) % count) for source in range(count)]
    return lax.ppermute(value, SUB, pairs)


def swap(value, count):
    pairs = [(source, source ^ 1) for source in range(count)]
    return lax.ppermute(value, SUB, pairs)


def swap_cores(value, core):
    sent = jnp.broadcast_to(value[None], (SIZES[-1],) + value.shape)
    got = lax.all_to_all(sent, SUB[-1], 0, 0, tiled=False)
    return lax.dynamic_index_in_dim(got, 1 - core, 0, keepdims=False)


def tile_order():
    y, z, x, c, i = np.meshgrid(
        *[np.arange(n) for n in SIZES], np.arange(TT), indexing="ij"
    )
    flat = (((y * SIZES[1] + z) * SIZES[2] + x) * SIZES[3] + c) * TT + i
    perm = [SUB.index(a) for a in RS_ORDER] + [4]
    return flat.transpose(perm).reshape(-1).astype(np.int32)


def body(records, green, pair_mask, tile_lists, tile_weights, tile_green):
    count = int(np.prod(SIZES))
    rec = records.astype(jnp.float32)
    grn = green.astype(jnp.float32)
    rec_real, rec_imag = (rec[:, :F], rec[:, F:])
    green_real, green_imag = (grn[:, :F], grn[:, F:])
    both = jnp.concatenate(
        [
            rec_real * green_real + rec_imag * green_imag,
            rec_real * green_imag - rec_imag * green_real,
            green_real * green_real + green_imag * green_imag,
        ],
        axis=1,
    ).astype(jnp.bfloat16)
    mask_bf = pair_mask.astype(jnp.bfloat16)
    core = lax.axis_index(SUB) % 2
    first = core == 0

    def cols(offset):
        return mask_bf[:, offset * C : (offset + 1) * C]

    def picked(on_first, on_second):
        return jnp.where(first, cols(on_first), cols(on_second))

    def add(total, columns, moving):
        return total + jnp.dot(columns, moving, preferred_element_type=jnp.float32)

    lists = jnp.concatenate([tile_lists, swap(tile_lists, count)], axis=0)
    weights = jnp.concatenate([tile_weights, swap(tile_weights, count)], axis=0)
    ahead = shifted(both, -2, count)
    behind = shifted(both, 2, count)
    ahead2 = shifted(ahead, -2, count)
    behind2 = shifted(behind, 2, count)
    total = jnp.dot(cols(HALF), both, preferred_element_type=jnp.float32)
    total = add(total, cols(HALF + 2), ahead)
    total = add(total, cols(HALF - 2), behind)
    tile_ids = jnp.asarray(tile_order()[: TT * count // SIZES[-1]]) + TT * (
        lax.axis_index(SUB) % 2
    )
    onehot = (lists[None, :, :] == tile_ids[:, None, None]).astype(jnp.float32)
    tile_map = jnp.sum(onehot * weights[None, :, :], axis=2)
    total, tile_map = lax.optimization_barrier((total, tile_map))
    swapped = swap_cores(jnp.concatenate([both, ahead, behind], axis=0), core)
    columns = [picked(HALF + 1, HALF - 1), picked(HALF + 3, HALF + 1), picked(HALF - 1, HALF - 3)]
    total = add(total, jnp.concatenate(columns, axis=1), swapped)
    last = swap_cores(jnp.where(first, ahead2, behind2), core)
    columns = [cols(HALF + 4), cols(HALF - 4), picked(HALF - 3, HALF + 3)]
    stacked = jnp.concatenate([ahead2, behind2, last], axis=0)
    total = add(total, jnp.concatenate(columns, axis=1), stacked)
    factor = 1.0 / jnp.sqrt(jnp.float32(WIN * C))
    total = total * factor
    q_real, q_imag, psum = (total[:, :F], total[:, F : 2 * F], total[:, 2 * F :])
    adj_real = rec_real * q_real - rec_imag * q_imag - green_real * psum
    adj_imag = rec_real * q_imag + rec_imag * q_real - green_imag * psum
    adjoint = jnp.concatenate([adj_real, adj_imag], axis=1).astype(jnp.bfloat16)
    response = jnp.dot(adjoint, tile_green, preferred_element_type=jnp.float32)
    responses = jnp.concatenate([response, swap_cores(response, core)], axis=0)
    part = jnp.dot(tile_map, responses, precision=lax.Precision.HIGHEST)
    for group in STAGES:
        ways = int(np.prod([SIZES[SUB.index(a)] for a in group]))
        part = part.reshape(ways, -1, part.shape[1])
        part = jnp.sum(lax.all_to_all(part, group, 0, 0, tiled=False), axis=0)
    return (adjoint, part)


def solution(mesh):
    devices = np.asarray(mesh.devices).reshape(SIZES)
    grid = Mesh(devices, SUB)
    rows = P(SUB, None)
    return jax.shard_map(
        body,
        mesh=grid,
        in_specs=(rows,) * 6,
        out_specs=(rows, rows),
        check_vma=False,
    )
```

```python
import numpy as np
import jax
import jax.numpy as jnp
from jax import lax
from jax.sharding import Mesh
from jax.sharding import PartitionSpec as P

C = 80
F = 1024
TT = 4
HALF = 4
WIN = 9

SUB = ("y", "z", "x", "c")
SIZES = (4, 4, 8, 2)
RS_ORDER = ("c", "x", "z", "y")
STAGES = (("x",), ("z", "y"))


def shifted(value, steps, count):
    pairs = [(source, (source + steps) % count) for source in range(count)]
    return lax.ppermute(value, SUB, pairs)


def swap(value, count):
    pairs = [(source, source ^ 1) for source in range(count)]
    return lax.ppermute(value, SUB, pairs)


def tile_order():
    y, z, x, c, i = np.meshgrid(
        *[np.arange(n) for n in SIZES], np.arange(TT), indexing="ij"
    )
    flat = (((y * SIZES[1] + z) * SIZES[2] + x) * SIZES[3] + c) * TT + i
    perm = [SUB.index(a) for a in RS_ORDER] + [4]
    return flat.transpose(perm).reshape(-1).astype(np.int32)


def body(records, green, pair_mask, tile_lists, tile_weights, tile_green):
    count = int(np.prod(SIZES))
    rec = records.astype(jnp.float32)
    grn = green.astype(jnp.float32)
    rec_real, rec_imag = (rec[:, :F], rec[:, F:])
    green_real, green_imag = (grn[:, :F], grn[:, F:])
    d_real, d_imag = (records[:, :F], records[:, F:])
    g_real, g_imag = (green[:, :F], green[:, F:])
    wide = lambda parts: jnp.concatenate(parts, axis=1).astype(jnp.float32)
    a = wide([d_real, d_real, g_real])
    b = wide([g_real, g_imag, g_real])
    c = wide([d_imag, -d_imag, g_imag])
    d = wide([g_imag, g_real, g_imag])
    both = (a * b + c * d).astype(jnp.bfloat16)
    mask_bf = pair_mask.astype(jnp.bfloat16)
    first = lax.axis_index(SUB) % 2 == 0

    def cols(offset):
        return mask_bf[:, offset * C : (offset + 1) * C]

    def picked(on_first, on_second):
        return jnp.where(first, cols(on_first), cols(on_second))

    def add(total, columns, moving):
        return total + jnp.dot(columns, moving, preferred_element_type=jnp.float32)

    lists = jnp.concatenate([tile_lists, swap(tile_lists, count)], axis=0)
    weights = jnp.concatenate([tile_weights, swap(tile_weights, count)], axis=0)
    ahead = shifted(both, -2, count)
    behind = shifted(both, 2, count)
    ahead2 = shifted(ahead, -2, count)
    behind2 = shifted(behind, 2, count)
    total = jnp.dot(cols(HALF), both, preferred_element_type=jnp.float32)
    total = add(total, cols(HALF + 2), ahead)
    total = add(total, cols(HALF - 2), behind)
    tile_ids = jnp.asarray(tile_order()[: TT * count // SIZES[-1]]) + TT * (
        lax.axis_index(SUB) % 2
    )
    onehot = (lists[None, :, :] == tile_ids[:, None, None]).astype(jnp.float32)
    tile_map = jnp.sum(onehot * weights[None, :, :], axis=2)
    total, tile_map = lax.optimization_barrier((total, tile_map))
    swapped = swap(jnp.concatenate([both, ahead, behind], axis=0), count)
    columns = [picked(HALF + 1, HALF - 1), picked(HALF + 3, HALF + 1), picked(HALF - 1, HALF - 3)]
    total = add(total, jnp.concatenate(columns, axis=1), swapped)
    last = swap(jnp.where(first, ahead2, behind2), count)
    columns = [cols(HALF + 4), cols(HALF - 4), picked(HALF - 3, HALF + 3)]
    stacked = jnp.concatenate([ahead2, behind2, last], axis=0)
    total = add(total, jnp.concatenate(columns, axis=1), stacked)
    factor = 1.0 / jnp.sqrt(jnp.float32(WIN * C))
    total = total * factor
    q_real, q_imag, psum = (total[:, :F], total[:, F : 2 * F], total[:, 2 * F :])
    adj_real = rec_real * q_real - rec_imag * q_imag - green_real * psum
    adj_imag = rec_real * q_imag + rec_imag * q_real - green_imag * psum
    adjoint = jnp.concatenate([adj_real, adj_imag], axis=1).astype(jnp.bfloat16)
    response = jnp.dot(adjoint, tile_green, preferred_element_type=jnp.float32)
    responses = jnp.concatenate([response, swap(response, count)], axis=0)
    part = jnp.dot(tile_map, responses, precision=lax.Precision.HIGHEST)
    for group in STAGES:
        ways = int(np.prod([SIZES[SUB.index(a)] for a in group]))
        part = part.reshape(ways, -1, part.shape[1])
        part = jnp.sum(lax.all_to_all(part, group, 0, 0, tiled=False), axis=0)
    return (adjoint, part)


def solution(mesh):
    devices = np.asarray(mesh.devices).reshape(SIZES)
    grid = Mesh(devices, SUB)
    rows = P(SUB, None)
    return jax.shard_map(
        body,
        mesh=grid,
        in_specs=(rows,) * 6,
        out_specs=(rows, rows),
        check_vma=False,
    )
```

```python
import numpy as np
import jax
import jax.numpy as jnp
from jax import lax
from jax.sharding import Mesh
from jax.sharding import PartitionSpec as P

C = 80
F = 1024
TT = 4
HALF = 4
WIN = 9

SUB = ("y", "z", "x", "c")
SIZES = (4, 4, 8, 2)
RS_ORDER = ("c", "x", "z", "y")
STAGES = (("x",), ("z", "y"))


def shifted(value, steps, count):
    pairs = [(source, (source + steps) % count) for source in range(count)]
    return lax.ppermute(value, SUB, pairs)


def swap(value, count):
    pairs = [(source, source ^ 1) for source in range(count)]
    return lax.ppermute(value, SUB, pairs)


def tile_order():
    y, z, x, c, i = np.meshgrid(
        *[np.arange(n) for n in SIZES], np.arange(TT), indexing="ij"
    )
    flat = (((y * SIZES[1] + z) * SIZES[2] + x) * SIZES[3] + c) * TT + i
    perm = [SUB.index(a) for a in RS_ORDER] + [4]
    return flat.transpose(perm).reshape(-1).astype(np.int32)


def body(records, green, pair_mask, tile_lists, tile_weights, tile_green):
    count = int(np.prod(SIZES))
    rec = records.astype(jnp.float32)
    grn = green.astype(jnp.float32)
    rec_real, rec_imag = (rec[:, :F], rec[:, F:])
    green_real, green_imag = (grn[:, :F], grn[:, F:])
    d_real, d_imag = (records[:, :F], records[:, F:])
    g_real, g_imag = (green[:, :F], green[:, F:])
    wide = lambda parts: jnp.concatenate(parts, axis=1).astype(jnp.float32)
    a = wide([d_real, d_real, g_real])
    b = wide([g_real, g_imag, g_real])
    c = wide([d_imag, -d_imag, g_imag])
    d = wide([g_imag, g_real, g_imag])
    both = (a * b + c * d).astype(jnp.bfloat16)
    mask_bf = pair_mask.astype(jnp.bfloat16)
    first = lax.axis_index(SUB) % 2 == 0

    def cols(offset):
        return mask_bf[:, offset * C : (offset + 1) * C]

    def picked(on_first, on_second):
        return jnp.where(first, cols(on_first), cols(on_second))

    def add(total, columns, moving):
        return total + jnp.dot(columns, moving, preferred_element_type=jnp.float32)

    lists = jnp.concatenate([tile_lists, swap(tile_lists, count)], axis=0)
    weights = jnp.concatenate([tile_weights, swap(tile_weights, count)], axis=0)
    ahead = shifted(both, -2, count)
    behind = shifted(both, 2, count)
    ahead2 = shifted(ahead, -2, count)
    behind2 = shifted(behind, 2, count)
    total = jnp.dot(cols(HALF), both, preferred_element_type=jnp.float32)
    total = add(total, cols(HALF + 2), ahead)
    total = add(total, cols(HALF - 2), behind)
    tile_ids = jnp.asarray(tile_order()[: TT * count // SIZES[-1]]) + TT * (
        lax.axis_index(SUB) % 2
    )
    onehot = (lists[None, :, :] == tile_ids[:, None, None]).astype(jnp.float32)
    tile_map = jnp.sum(onehot * weights[None, :, :], axis=2)
    total, tile_map = lax.optimization_barrier((total, tile_map))
    swapped = swap(jnp.concatenate([both, ahead, behind], axis=0), count)
    columns = [picked(HALF + 1, HALF - 1), picked(HALF + 3, HALF + 1), picked(HALF - 1, HALF - 3)]
    total = add(total, jnp.concatenate(columns, axis=1), swapped)
    last = swap(jnp.where(first, ahead2, behind2), count)
    columns = [cols(HALF + 4), cols(HALF - 4), picked(HALF - 3, HALF + 3)]
    stacked = jnp.concatenate([ahead2, behind2, last], axis=0)
    total = add(total, jnp.concatenate(columns, axis=1), stacked)
    factor = 1.0 / jnp.sqrt(jnp.float32(WIN * C))
    total = total * factor
    q_real, q_imag, psum = (total[:, :F], total[:, F : 2 * F], total[:, 2 * F :])
    adj_real = rec_real * q_real - rec_imag * q_imag - green_real * psum
    adj_imag = rec_real * q_imag + rec_imag * q_real - green_imag * psum
    adjoint = jnp.concatenate([adj_real, adj_imag], axis=1).astype(jnp.bfloat16)
    response = jnp.dot(adjoint, tile_green, preferred_element_type=jnp.float32)
    part = jnp.dot(tile_map[:, :C], response, precision=lax.Precision.HIGHEST)
    partner = swap(response, count)
    part = part + jnp.dot(tile_map[:, C:], partner, precision=lax.Precision.HIGHEST)
    for group in STAGES:
        ways = int(np.prod([SIZES[SUB.index(a)] for a in group]))
        part = part.reshape(ways, -1, part.shape[1])
        part = jnp.sum(lax.all_to_all(part, group, 0, 0, tiled=False), axis=0)
    return (adjoint, part)


def solution(mesh):
    devices = np.asarray(mesh.devices).reshape(SIZES)
    grid = Mesh(devices, SUB)
    rows = P(SUB, None)
    return jax.shard_map(
        body,
        mesh=grid,
        in_specs=(rows,) * 6,
        out_specs=(rows, rows),
        check_vma=False,
    )
```

```python
import numpy as np
import jax
import jax.numpy as jnp
from jax import lax
from jax.sharding import Mesh
from jax.sharding import PartitionSpec as P

C = 80
F = 1024
TT = 4
HALF = 4
WIN = 9

SUB = ("y", "z", "x", "c")
SIZES = (4, 4, 8, 2)
RS_ORDER = ("c", "x", "z", "y")
STAGES = (("x",), ("z", "y"))


def shifted(value, steps, count):
    pairs = [(source, (source + steps) % count) for source in range(count)]
    return lax.ppermute(value, SUB, pairs)


def swap(value, count):
    pairs = [(source, source ^ 1) for source in range(count)]
    return lax.ppermute(value, SUB, pairs)


def across(value, count):
    pairs = [(s, s - 1 if s % 2 == 0 else s + 1) for s in range(count)]
    return lax.ppermute(value, SUB, [(s, t % count) for s, t in pairs])


def tile_order():
    y, z, x, c, i = np.meshgrid(
        *[np.arange(n) for n in SIZES], np.arange(TT), indexing="ij"
    )
    flat = (((y * SIZES[1] + z) * SIZES[2] + x) * SIZES[3] + c) * TT + i
    perm = [SUB.index(a) for a in RS_ORDER] + [4]
    return flat.transpose(perm).reshape(-1).astype(np.int32)


def body(records, green, pair_mask, tile_lists, tile_weights, tile_green):
    count = int(np.prod(SIZES))
    rec = records.astype(jnp.float32)
    grn = green.astype(jnp.float32)
    rec_real, rec_imag = (rec[:, :F], rec[:, F:])
    green_real, green_imag = (grn[:, :F], grn[:, F:])
    both = jnp.concatenate(
        [
            rec_real * green_real + rec_imag * green_imag,
            rec_real * green_imag - rec_imag * green_real,
            green_real * green_real + green_imag * green_imag,
        ],
        axis=1,
    ).astype(jnp.bfloat16)
    mask_bf = pair_mask.astype(jnp.bfloat16)
    first = lax.axis_index(SUB) % 2 == 0

    def cols(offset):
        return mask_bf[:, offset * C : (offset + 1) * C]

    def picked(on_first, on_second):
        return jnp.where(first, cols(on_first), cols(on_second))

    def add(total, columns, moving):
        return total + jnp.dot(columns, moving, preferred_element_type=jnp.float32)

    lists = jnp.concatenate([tile_lists, swap(tile_lists, count)], axis=0)
    weights = jnp.concatenate([tile_weights, swap(tile_weights, count)], axis=0)
    ahead = shifted(both, -2, count)
    behind = shifted(both, 2, count)
    ahead2 = shifted(ahead, -2, count)
    behind2 = shifted(behind, 2, count)
    last = across(jnp.where(first, ahead, behind), count)
    total = jnp.dot(cols(HALF), both, preferred_element_type=jnp.float32)
    total = add(total, cols(HALF + 2), ahead)
    total = add(total, cols(HALF - 2), behind)
    tile_ids = jnp.asarray(tile_order()[: TT * count // SIZES[-1]]) + TT * (
        lax.axis_index(SUB) % 2
    )
    onehot = (lists[None, :, :] == tile_ids[:, None, None]).astype(jnp.float32)
    tile_map = jnp.sum(onehot * weights[None, :, :], axis=2)
    total, tile_map = lax.optimization_barrier((total, tile_map))
    swapped = swap(jnp.concatenate([both, ahead, behind], axis=0), count)
    columns = [picked(HALF + 1, HALF - 1), picked(HALF + 3, HALF + 1), picked(HALF - 1, HALF - 3)]
    total = add(total, jnp.concatenate(columns, axis=1), swapped)
    columns = [cols(HALF + 4), cols(HALF - 4), picked(HALF - 3, HALF + 3)]
    stacked = jnp.concatenate([ahead2, behind2, last], axis=0)
    total = add(total, jnp.concatenate(columns, axis=1), stacked)
    factor = 1.0 / jnp.sqrt(jnp.float32(WIN * C))
    total = total * factor
    q_real, q_imag, psum = (total[:, :F], total[:, F : 2 * F], total[:, 2 * F :])
    adj_real = rec_real * q_real - rec_imag * q_imag - green_real * psum
    adj_imag = rec_real * q_imag + rec_imag * q_real - green_imag * psum
    adjoint = jnp.concatenate([adj_real, adj_imag], axis=1).astype(jnp.bfloat16)
    response = jnp.dot(adjoint, tile_green, preferred_element_type=jnp.float32)
    responses = jnp.concatenate([response, swap(response, count)], axis=0)
    part = jnp.dot(tile_map, responses, precision=lax.Precision.HIGHEST)
    for group in STAGES:
        ways = int(np.prod([SIZES[SUB.index(a)] for a in group]))
        part = part.reshape(ways, -1, part.shape[1])
        part = jnp.sum(lax.all_to_all(part, group, 0, 0, tiled=False), axis=0)
    return (adjoint, part)


def solution(mesh):
    devices = np.asarray(mesh.devices).reshape(SIZES)
    grid = Mesh(devices, SUB)
    rows = P(SUB, None)
    return jax.shard_map(
        body,
        mesh=grid,
        in_specs=(rows,) * 6,
        out_specs=(rows, rows),
        check_vma=False,
    )
```

```python
import numpy as np
import jax
import jax.numpy as jnp
from jax import lax
from jax.sharding import Mesh
from jax.sharding import PartitionSpec as P

C = 80
F = 1024
TT = 4
HALF = 4
WIN = 9

SUB = ("y", "z", "x", "c")
SIZES = (4, 4, 8, 2)
RS_ORDER = ("c", "x", "z", "y")
STAGES = (("x",), ("z", "y"))


def shifted(value, steps, count):
    pairs = [(source, (source + steps) % count) for source in range(count)]
    return lax.ppermute(value, SUB, pairs)


def swap(value, count):
    pairs = [(source, source ^ 1) for source in range(count)]
    return lax.ppermute(value, SUB, pairs)


def tile_order():
    y, z, x, c, i = np.meshgrid(
        *[np.arange(n) for n in SIZES], np.arange(TT), indexing="ij"
    )
    flat = (((y * SIZES[1] + z) * SIZES[2] + x) * SIZES[3] + c) * TT + i
    perm = [SUB.index(a) for a in RS_ORDER] + [4]
    return flat.transpose(perm).reshape(-1).astype(np.int32)


def body(records, green, pair_mask, tile_lists, tile_weights, tile_green):
    count = int(np.prod(SIZES))
    rec = records.astype(jnp.float32)
    grn = green.astype(jnp.float32)
    rec_real, rec_imag = (rec[:, :F], rec[:, F:])
    green_real, green_imag = (grn[:, :F], grn[:, F:])
    both = jnp.concatenate(
        [
            rec_real * green_real + rec_imag * green_imag,
            rec_real * green_imag - rec_imag * green_real,
            green_real * green_real + green_imag * green_imag,
        ],
        axis=1,
    ).astype(jnp.bfloat16)
    mask_bf = pair_mask.astype(jnp.bfloat16)
    first = lax.axis_index(SUB) % 2 == 0

    def cols(offset):
        return mask_bf[:, offset * C : (offset + 1) * C]

    def picked(on_first, on_second):
        return jnp.where(first, cols(on_first), cols(on_second))

    def add(total, columns, moving):
        return total + jnp.dot(columns, moving, preferred_element_type=jnp.float32)

    lists = jnp.concatenate([tile_lists, swap(tile_lists, count)], axis=0)
    weights = jnp.concatenate([tile_weights, swap(tile_weights, count)], axis=0)
    ahead = shifted(both, -2, count)
    behind = shifted(both, 2, count)
    ahead2 = shifted(ahead, -2, count)
    behind2 = shifted(behind, 2, count)
    total = jnp.dot(cols(HALF), both, preferred_element_type=jnp.float32)
    total = add(total, cols(HALF + 2), ahead)
    total = add(total, cols(HALF - 2), behind)
    tile_ids = jnp.asarray(tile_order()[: TT * count // SIZES[-1]]) + TT * (
        lax.axis_index(SUB) % 2
    )
    onehot = (lists[None, :, :] == tile_ids[:, None, None]).astype(jnp.float32)
    tile_map = jnp.sum(onehot * weights[None, :, :], axis=2)
    total, tile_map = lax.optimization_barrier((total, tile_map))
    swapped = swap(jnp.concatenate([both, ahead, behind], axis=0), count)
    columns = [picked(HALF + 1, HALF - 1), picked(HALF + 3, HALF + 1), picked(HALF - 1, HALF - 3)]
    total = add(total, jnp.concatenate(columns, axis=1), swapped)
    last = swap(jnp.where(first, ahead2, behind2), count)
    columns = [cols(HALF + 4), cols(HALF - 4), picked(HALF - 3, HALF + 3)]
    stacked = jnp.concatenate([ahead2, behind2, last], axis=0)
    total = add(total, jnp.concatenate(columns, axis=1), stacked)
    factor = 1.0 / jnp.sqrt(jnp.float32(WIN * C))
    total = total * factor
    q_real, q_imag, psum = (total[:, :F], total[:, F : 2 * F], total[:, 2 * F :])
    adj_real = rec_real * q_real - rec_imag * q_imag - green_real * psum
    adj_imag = rec_real * q_imag + rec_imag * q_real - green_imag * psum
    adjoint = jnp.concatenate([adj_real, adj_imag], axis=1).astype(jnp.bfloat16)
    response = jnp.dot(adjoint, tile_green, preferred_element_type=jnp.float32)
    responses = jnp.concatenate([response, swap(response, count)], axis=0)
    part = jnp.dot(tile_map, responses, precision=lax.Precision.HIGH)
    for group in STAGES:
        ways = int(np.prod([SIZES[SUB.index(a)] for a in group]))
        part = part.reshape(ways, -1, part.shape[1])
        part = jnp.sum(lax.all_to_all(part, group, 0, 0, tiled=False), axis=0)
    return (adjoint, part)


def solution(mesh):
    devices = np.asarray(mesh.devices).reshape(SIZES)
    grid = Mesh(devices, SUB)
    rows = P(SUB, None)
    return jax.shard_map(
        body,
        mesh=grid,
        in_specs=(rows,) * 6,
        out_specs=(rows, rows),
        check_vma=False,
    )
```

```python
import numpy as np
import jax
import jax.numpy as jnp
from jax import lax
from jax.sharding import Mesh
from jax.sharding import PartitionSpec as P

C = 80
F = 1024
TT = 4
HALF = 4
WIN = 9

SUB = ("y", "z", "x", "c")
SIZES = (4, 4, 8, 2)
RS_ORDER = ("c", "x", "z", "y")
STAGES = (("x",), ("z", "y"))


def shifted(value, steps, count):
    pairs = [(source, (source + steps) % count) for source in range(count)]
    return lax.ppermute(value, SUB, pairs)


def swap(value, count):
    pairs = [(source, source ^ 1) for source in range(count)]
    return lax.ppermute(value, SUB, pairs)


def tile_order():
    y, z, x, c, i = np.meshgrid(
        *[np.arange(n) for n in SIZES], np.arange(TT), indexing="ij"
    )
    flat = (((y * SIZES[1] + z) * SIZES[2] + x) * SIZES[3] + c) * TT + i
    perm = [SUB.index(a) for a in RS_ORDER] + [4]
    return flat.transpose(perm).reshape(-1).astype(np.int32)


def body(records, green, pair_mask, tile_lists, tile_weights, tile_green):
    count = int(np.prod(SIZES))
    rec = records.astype(jnp.float32)
    grn = green.astype(jnp.float32)
    rec_real, rec_imag = (rec[:, :F], rec[:, F:])
    green_real, green_imag = (grn[:, :F], grn[:, F:])
    both = jnp.concatenate(
        [
            rec_real * green_real + rec_imag * green_imag,
            rec_real * green_imag - rec_imag * green_real,
            green_real * green_real + green_imag * green_imag,
        ],
        axis=1,
    ).astype(jnp.bfloat16)
    mask_bf = pair_mask.astype(jnp.bfloat16)
    first = lax.axis_index(SUB) % 2 == 0

    def cols(offset):
        return mask_bf[:, offset * C : (offset + 1) * C]

    def picked(on_first, on_second):
        return jnp.where(first, cols(on_first), cols(on_second))

    def add(total, columns, moving):
        return total + jnp.dot(columns, moving, preferred_element_type=jnp.float32)

    lists = jnp.concatenate([tile_lists, swap(tile_lists, count)], axis=0)
    weights = jnp.concatenate([tile_weights, swap(tile_weights, count)], axis=0)
    ahead = shifted(both, -2, count)
    behind = shifted(both, 2, count)
    ahead2 = shifted(ahead, -2, count)
    behind2 = shifted(behind, 2, count)
    total = jnp.dot(cols(HALF), both, preferred_element_type=jnp.float32)
    total = add(total, cols(HALF + 2), ahead)
    total = add(total, cols(HALF - 2), behind)
    tile_ids = jnp.asarray(tile_order()[: TT * count // SIZES[-1]]) + TT * (
        lax.axis_index(SUB) % 2
    )
    onehot = (lists[None, :, :] == tile_ids[:, None, None]).astype(jnp.float32)
    tile_map = jnp.sum(onehot * weights[None, :, :], axis=2)
    total, tile_map = lax.optimization_barrier((total, tile_map))
    swapped = swap(jnp.concatenate([both, ahead, behind], axis=0), count)
    columns = [picked(HALF + 1, HALF - 1), picked(HALF + 3, HALF + 1), picked(HALF - 1, HALF - 3)]
    total = add(total, jnp.concatenate(columns, axis=1), swapped)
    last = swap(jnp.where(first, ahead2, behind2), count)
    columns = [cols(HALF + 4), cols(HALF - 4), picked(HALF - 3, HALF + 3)]
    stacked = jnp.concatenate([ahead2, behind2, last], axis=0)
    total = add(total, jnp.concatenate(columns, axis=1), stacked)
    factor = 1.0 / jnp.sqrt(jnp.float32(WIN * C))
    total = total * factor
    q_real, q_imag, psum = (total[:, :F], total[:, F : 2 * F], total[:, 2 * F :])
    adj_real = rec_real * q_real - rec_imag * q_imag - green_real * psum
    adj_imag = rec_real * q_imag + rec_imag * q_real - green_imag * psum
    adjoint = jnp.concatenate([adj_real, adj_imag], axis=1).astype(jnp.bfloat16)
    response = jnp.dot(adjoint, tile_green, preferred_element_type=jnp.float32)
    responses = jnp.concatenate([response, swap(response, count)], axis=0)
    part = jnp.dot(tile_map, responses, precision=lax.Precision.HIGH)
    width = part.shape[1]
    for group in STAGES:
        ways = int(np.prod([SIZES[SUB.index(a)] for a in group]))
        rows = part.shape[0] // ways
        fold = 8 // rows if rows < 8 else 1
        part = part.reshape(ways, rows * fold, width // fold)
        part = jnp.sum(lax.all_to_all(part, group, 0, 0, tiled=False), axis=0)
        part = part.reshape(rows, width)
    return (adjoint, part)


def solution(mesh):
    devices = np.asarray(mesh.devices).reshape(SIZES)
    grid = Mesh(devices, SUB)
    rows = P(SUB, None)
    return jax.shard_map(
        body,
        mesh=grid,
        in_specs=(rows,) * 6,
        out_specs=(rows, rows),
        check_vma=False,
    )
```

```python
import numpy as np
import jax
import jax.numpy as jnp
from jax import lax
from jax.sharding import Mesh
from jax.sharding import PartitionSpec as P

C = 80
F = 1024
TT = 4
HALF = 4
WIN = 9

SUB = ("y", "z", "x", "c")
SIZES = (4, 4, 8, 2)
RS_ORDER = ("c", "x", "z", "y")
STAGES = (("x",), ("z", "y"))


def shifted(value, steps, count):
    pairs = [(source, (source + steps) % count) for source in range(count)]
    return lax.ppermute(value, SUB, pairs)


def swap(value, count):
    pairs = [(source, source ^ 1) for source in range(count)]
    return lax.ppermute(value, SUB, pairs)


def tile_order():
    y, z, x, c, i = np.meshgrid(
        *[np.arange(n) for n in SIZES], np.arange(TT), indexing="ij"
    )
    flat = (((y * SIZES[1] + z) * SIZES[2] + x) * SIZES[3] + c) * TT + i
    perm = [SUB.index(a) for a in RS_ORDER] + [4]
    return flat.transpose(perm).reshape(-1).astype(np.int32)


def body(records, green, pair_mask, tile_lists, tile_weights, tile_green):
    count = int(np.prod(SIZES))
    rec = records.astype(jnp.float32)
    grn = green.astype(jnp.float32)
    rec_real, rec_imag = (rec[:, :F], rec[:, F:])
    green_real, green_imag = (grn[:, :F], grn[:, F:])
    both = jnp.concatenate(
        [
            rec_real * green_real + rec_imag * green_imag,
            rec_real * green_imag - rec_imag * green_real,
            green_real * green_real + green_imag * green_imag,
        ],
        axis=1,
    ).astype(jnp.bfloat16)
    mask_bf = pair_mask.astype(jnp.bfloat16)
    first = lax.axis_index(SUB) % 2 == 0

    def cols(offset):
        return mask_bf[:, offset * C : (offset + 1) * C]

    def picked(on_first, on_second):
        return jnp.where(first, cols(on_first), cols(on_second))

    def add(total, columns, moving):
        return total + jnp.dot(columns, moving, preferred_element_type=jnp.float32)

    listed = jnp.concatenate([tile_lists.astype(jnp.float32), tile_weights], axis=1)
    listed = jnp.concatenate([listed, swap(listed, count)], axis=0)
    lists, weights = (listed[:, : tile_lists.shape[1]], listed[:, tile_lists.shape[1] :])
    ahead = shifted(both, -2, count)
    behind = shifted(both, 2, count)
    ahead2 = shifted(ahead, -2, count)
    behind2 = shifted(behind, 2, count)
    total = jnp.dot(cols(HALF), both, preferred_element_type=jnp.float32)
    total = add(total, cols(HALF + 2), ahead)
    total = add(total, cols(HALF - 2), behind)
    tile_ids = jnp.asarray(tile_order()[: TT * count // SIZES[-1]]) + TT * (
        lax.axis_index(SUB) % 2
    )
    tile_ids = tile_ids.astype(jnp.float32)
    onehot = (lists[None, :, :] == tile_ids[:, None, None]).astype(jnp.float32)
    tile_map = jnp.sum(onehot * weights[None, :, :], axis=2)
    total, tile_map = lax.optimization_barrier((total, tile_map))
    swapped = swap(jnp.concatenate([both, ahead, behind], axis=0), count)
    columns = [picked(HALF + 1, HALF - 1), picked(HALF + 3, HALF + 1), picked(HALF - 1, HALF - 3)]
    total = add(total, jnp.concatenate(columns, axis=1), swapped)
    last = swap(jnp.where(first, ahead2, behind2), count)
    columns = [cols(HALF + 4), cols(HALF - 4), picked(HALF - 3, HALF + 3)]
    stacked = jnp.concatenate([ahead2, behind2, last], axis=0)
    total = add(total, jnp.concatenate(columns, axis=1), stacked)
    factor = 1.0 / jnp.sqrt(jnp.float32(WIN * C))
    total = total * factor
    q_real, q_imag, psum = (total[:, :F], total[:, F : 2 * F], total[:, 2 * F :])
    adj_real = rec_real * q_real - rec_imag * q_imag - green_real * psum
    adj_imag = rec_real * q_imag + rec_imag * q_real - green_imag * psum
    adjoint = jnp.concatenate([adj_real, adj_imag], axis=1).astype(jnp.bfloat16)
    response = jnp.dot(adjoint, tile_green, preferred_element_type=jnp.float32)
    responses = jnp.concatenate([response, swap(response, count)], axis=0)
    part = jnp.dot(tile_map, responses, precision=lax.Precision.HIGH)
    for group in STAGES:
        ways = int(np.prod([SIZES[SUB.index(a)] for a in group]))
        part = part.reshape(ways, -1, part.shape[1])
        part = jnp.sum(lax.all_to_all(part, group, 0, 0, tiled=False), axis=0)
    return (adjoint, part)


def solution(mesh):
    devices = np.asarray(mesh.devices).reshape(SIZES)
    grid = Mesh(devices, SUB)
    rows = P(SUB, None)
    return jax.shard_map(
        body,
        mesh=grid,
        in_specs=(rows,) * 6,
        out_specs=(rows, rows),
        check_vma=False,
    )
```
